32 devices in a mesh: layer: 4 (over x, core), tok: 8 (over z, y).
Axes of the slice: x: 2, y: 2, z: 4, core: 2. Of those that a mesh axis runs over, the one named last changes fastest.
Arguments:
- active_codes: bfloat16 [4, 1024, 32], P('layer', 'tok'), may hold values from 0.19921875 to 3
- latent_ids: int32 [4, 1024, 32], P('layer', 'tok'), may hold values from 0 to 32767, as said below
- decoder: bfloat16 [4, 32768, 4096], P('layer', 'tok'), may hold values from -1 to 1
- carry_gain: float32 [4, 4096], P('layer'), may hold values from 0.1 to 1
- earlier_sum: bfloat16 [1024, 4096], P('tok'), may hold values from -6 to 6
- targets: bfloat16 [4, 1024, 4096], P('layer', 'tok'), may hold values from -6 to 6
Outputs:
- reconstruction: bfloat16 [4, 1024, 4096], P('layer', 'tok')
- code_grad: float32 [4, 1024, 32], P('layer', 'tok')
The draws below stay inside these ranges and needn't reach their ends.
Inputs may be any that keep to these rules, and one draw needn't show every extreme that they name: `latent_ids`: A token's 32 ids in one layer are distinct. In each layer, the 128 tokens of one aligned block have at most 768 ids in any one range of 4096 consecutive latents, and in every layer one range holds exactly 768 ids of every block.
All inputs are finite; a program needn't handle non-finite values.
Results may differ from the reference program's by a relative error of at most 0.019.
Values may be sent and summed in bfloat16 or wider, within the bound.
No kernel may reach another device: no remote copies, remote signals or barrier semaphores. Data moves between devices by JAX's collectives and lax.ppermute only.
A program may use at most 256 MiB of HBM per device.

```python
import math
import jax
import jax.numpy as jnp
from jax import lax

D = 4096
LAT = 32768
K = 32
TOK_DEV = 128
WINDOW_LAYERS = 4
TOKENS = 1024
LAT_DEV = 4096
CAP = 768
N_TOK = 8


def draw_latent_ids(key, part):
    block_count = TOKENS // TOK_DEV
    per_block = TOK_DEV * K
    range_size = LAT // block_count
    hot_key, weight_key, perm_key, base_key = jax.random.split(key, 4)
    hottest = jax.random.randint(hot_key, (WINDOW_LAYERS, 1, 1), 0, block_count)
    ranges = jnp.arange(block_count, dtype=jnp.int32)
    is_hot = ranges[None, None, :] == hottest
    weights = jax.random.randint(weight_key, (WINDOW_LAYERS, block_count, block_count), 4, 6)
    weights = jnp.where(is_hot, 0, weights)
    leftover = per_block - CAP
    counts = leftover * weights // jnp.sum(weights, axis=-1, keepdims=True)
    remainder = leftover - jnp.sum(counts, axis=-1, keepdims=True)
    cold_index = ranges[None, None, :] - (ranges[None, None, :] > hottest).astype(jnp.int32)
    counts = counts + (~is_hot & (cold_index < remainder)).astype(jnp.int32)
    counts = jnp.where(is_hot, CAP, counts)

    def one_block(block_counts, block_key):
        listed = jnp.repeat(ranges, block_counts, total_repeat_length=per_block)
        return jax.random.permutation(block_key, listed)
    block_keys = jax.random.split(perm_key, WINDOW_LAYERS * block_count)
    owning = jax.vmap(one_block)(counts.reshape(WINDOW_LAYERS * block_count, block_count), block_keys)
    owning = owning.reshape(WINDOW_LAYERS, TOKENS, K).astype(jnp.int32)
    matching = owning[..., :, None] == owning[..., None, :]
    before = jnp.arange(K)[None, :] < jnp.arange(K)[:, None]
    within = jnp.sum((matching & before).astype(jnp.int32), axis=-1)
    offset = jax.random.randint(base_key, (WINDOW_LAYERS, TOKENS, 1), 0, range_size)
    inside = (offset + owning * 7 + within) % range_size
    return (owning * range_size + inside).astype(jnp.int32)


def draw_carry_gain(key, part):
    selection_key, quick_random_key, gradual_random_key, spike_random_key, depth_random_key = jax.random.split(key, 5)
    share = 0.5
    gradual_mask = jax.random.uniform(selection_key, (1, D)) < share
    quick_layer_gain = jax.random.uniform(quick_random_key, (WINDOW_LAYERS, D), minval=0.2, maxval=0.5)
    gradual_layer_gain = jax.random.uniform(gradual_random_key, (WINDOW_LAYERS, D), minval=0.85, maxval=1.0)
    spike_events = jax.random.uniform(spike_random_key, (WINDOW_LAYERS, 1)) < 0.25
    layer_depth = jax.random.uniform(depth_random_key, (WINDOW_LAYERS, 1), minval=0.5, maxval=0.8)
    return (jnp.where(gradual_mask, gradual_layer_gain, quick_layer_gain) * jnp.where(spike_events, layer_depth, 1.0)).astype(jnp.float32)


def level_of(key, dims, shards, smallest, largest):
    def one(dim, blocks):
        heights = jax.random.uniform(jax.random.fold_in(jax.random.fold_in(key, 6), dim), (blocks,), jnp.float32, smallest / len(shards), largest / len(shards))
        return jnp.repeat(jnp.exp(heights), dims[dim] // blocks).reshape((-1,) + (1,) * (len(dims) - dim - 1))

    loudness = one(*shards[0])
    for cut in shards[1:]:
        loudness = loudness * one(*cut)
    return loudness


def centred(own_key, shape, width, limit, cuts=(), held_as=jnp.bfloat16):
    gain = level_of(own_key, shape, cuts, -0.22, 0.18) if cuts else 1.0
    array = jax.random.normal(own_key, shape, jnp.float32) * width * gain
    return jnp.minimum(jnp.maximum(array, -limit), limit).astype(held_as)


def setup_inputs(seed: int = 0) -> dict:
    streams_of = jax.random.split(jax.random.key(seed), 7)
    active_codes = jnp.clip(jnp.exp(math.log(3.0) - 2.7119641 * jax.random.uniform(streams_of[0], (WINDOW_LAYERS, TOKENS, K), jnp.float32) ** level_of(streams_of[0], (WINDOW_LAYERS, TOKENS, K), ((0, 4), (1, 8)), -0.2, 0.2)), 0.19921875, 3.0).astype(jnp.bfloat16)
    latent_ids = draw_latent_ids(jax.random.fold_in(streams_of[6], 71), 0)
    decoder = centred(streams_of[2], (WINDOW_LAYERS, LAT, D), K ** -0.5, 1.0, ((0, 4), (1, 8)))
    carry_gain = draw_carry_gain(jax.random.fold_in(streams_of[6], 71), 0)
    earlier_sum = centred(streams_of[4], (TOKENS, D), 1.0, 6.0, ((0, 8),))
    targets = centred(streams_of[5], (WINDOW_LAYERS, TOKENS, D), 1.0, 6.0, ((0, 4), (1, 8)))
    return {"active_codes": active_codes, "latent_ids": latent_ids, "decoder": decoder, "carry_gain": carry_gain, "earlier_sum": earlier_sum, "targets": targets}


def layer_decode(weights, id_rows, code_rows):
    block_count = id_rows.shape[0] // TOK_DEV

    def one_block(pairing):
        block_ids, block_codes = pairing
        gathered = jnp.take(weights, block_ids, axis=0).astype(jnp.float32) * block_codes.astype(jnp.float32)[:, :, None]
        segment_ids = (jnp.arange(TOK_DEV, dtype=jnp.int32)[:, None] * N_TOK + block_ids // LAT_DEV).reshape(-1)
        range_sums = jax.ops.segment_sum(gathered.reshape(-1, D), segment_ids, num_segments=TOK_DEV * N_TOK)
        rounded = lax.optimization_barrier(range_sums.astype(jnp.bfloat16)).astype(jnp.float32)
        return jnp.sum(rounded.reshape(TOK_DEV, N_TOK, D), axis=1)

    blocks = lax.map(one_block, (id_rows.reshape(block_count, TOK_DEV, K), code_rows.reshape(block_count, TOK_DEV, K)))
    return blocks.reshape(block_count * TOK_DEV, D)


def layer_grads(weights, id_rows, grad_rows):
    block_count = id_rows.shape[0] // TOK_DEV

    def one_block(pairing):
        block_ids, block_grads = pairing
        gathered = jnp.take(weights, block_ids, axis=0).astype(jnp.float32)
        return jnp.einsum("tkd,td->tk", gathered, block_grads.astype(jnp.float32))

    blocks = lax.map(one_block, (id_rows.reshape(block_count, TOK_DEV, K), grad_rows.reshape(block_count, TOK_DEV, D)))
    return blocks.reshape(block_count * TOK_DEV, K)


def reference(active_codes, latent_ids, decoder, carry_gain, earlier_sum, targets):
    carried = earlier_sum.astype(jnp.float32)
    recon_list = []
    misfits = []
    for layer_pos in range(WINDOW_LAYERS):
        decoded = layer_decode(decoder[layer_pos], latent_ids[layer_pos], active_codes[layer_pos])
        carried = decoded + carry_gain[layer_pos][None, :] * carried
        recon_list.append(carried)
        misfits.append(carried - targets[layer_pos].astype(jnp.float32))
    grads = [misfits[WINDOW_LAYERS - 1]] * WINDOW_LAYERS
    running = misfits[WINDOW_LAYERS - 1]
    for layer_pos in range(WINDOW_LAYERS - 2, -1, -1):
        running = misfits[layer_pos] + carry_gain[layer_pos + 1][None, :] * running
        grads[layer_pos] = running
    code_list = []
    for layer_pos in range(WINDOW_LAYERS):
        code_list.append(layer_grads(decoder[layer_pos], latent_ids[layer_pos], grads[layer_pos].astype(jnp.bfloat16)))
    return jnp.stack(recon_list).astype(jnp.bfloat16), jnp.stack(code_list)
```

```python
import jax
import jax.numpy as jnp
from jax import lax
from jax.sharding import PartitionSpec as P

LANES = 128


def prefix(shard, axis, combine, identity, reverse):
    length, mine = (lax.axis_size(axis), lax.axis_index(axis))
    everything = jax.tree.map(
        lambda part, kind: lax.all_gather(part.astype(kind), axis),
        shard,
        (jnp.bfloat16, jnp.bfloat16),
    )
    start = jax.tree.map(
        lambda part, zero: jnp.broadcast_to(jnp.asarray(zero, part.dtype), part.shape),
        shard,
        identity,
    )

    def lap(k, before):
        at = length - 1 - k if reverse else k
        reached = at > mine if reverse else at < mine
        new = combine(
            before, jax.tree.map(lambda part, own: part[at].astype(own.dtype), everything, shard)
        )
        return jax.tree.map(lambda a, b: jnp.where(reached, a, b), new, before)

    return lax.fori_loop(0, length, lap, start)


def compose(earlier_part, later_part):
    return (earlier_part[0] * later_part[0], later_part[0] * earlier_part[1] + later_part[1])


def selectors(ids_all, range_size):
    base = lax.axis_index("tok") * range_size
    local = ids_all - base
    inside = (local >= 0) & (local < range_size)
    high = jnp.where(inside, local // LANES, -1)
    low = local % LANES
    high_hot = high[..., None] == jnp.arange(range_size // LANES, dtype=jnp.int32)
    low_hot = low[..., None] == jnp.arange(LANES, dtype=jnp.int32)
    return high_hot, low_hot


def on_device(active_codes, latent_ids, decoder, carry_gain, earlier_sum, targets):
    range_size = decoder.shape[1]
    weights = decoder[0]
    ids_all = lax.all_gather(latent_ids[0], "tok", axis=0, tiled=True)
    codes_all = lax.all_gather(active_codes[0], "tok", axis=0, tiled=True)
    tokens = ids_all.shape[0]
    high_hot, low_hot = selectors(ids_all, range_size)
    coded_high = jnp.where(high_hot, codes_all[..., None], jnp.zeros((), jnp.bfloat16))
    spread = jnp.einsum(
        "tkh,tkl->thl", coded_high, low_hot.astype(jnp.bfloat16), preferred_element_type=jnp.float32
    )
    spread = spread.astype(jnp.bfloat16).reshape(tokens, range_size)
    partial = jnp.dot(spread, weights, preferred_element_type=jnp.float32).astype(jnp.bfloat16)
    decoded = lax.psum_scatter(partial, "tok", scatter_dimension=0, tiled=True).astype(jnp.float32)
    identity = (jnp.ones_like(carry_gain), jnp.zeros_like(decoded))
    ahead_gain, ahead_sum = prefix((carry_gain, decoded), "layer", compose, identity, False)
    recon_full = carry_gain * (ahead_gain * earlier_sum.astype(jnp.float32) + ahead_sum) + decoded
    misfit = recon_full - targets[0].astype(jnp.float32)
    behind_gain, behind_sum = prefix(
        (carry_gain, carry_gain * misfit), "layer", compose, identity, True
    )
    grad_low = (misfit + behind_sum).astype(jnp.bfloat16)
    segment = lax.all_gather(grad_low, "tok", axis=0, tiled=True)
    products = lax.dot_general(
        segment, weights, (((1,), (1,)), ((), ())), preferred_element_type=jnp.float32
    )
    products = products.reshape(tokens, range_size // LANES, LANES)
    picked_low = jnp.einsum(
        "thl,tkl->tkh",
        products,
        low_hot.astype(jnp.float32),
        precision=lax.Precision.HIGHEST,
        preferred_element_type=jnp.float32,
    )
    partial_grad = jnp.sum(jnp.where(high_hot, picked_low, 0.0), axis=-1)
    code_grad = lax.psum_scatter(partial_grad, "tok", scatter_dimension=0, tiled=True)
    return (recon_full.astype(jnp.bfloat16)[None], code_grad[None])


def solution(mesh):
    return jax.shard_map(
        on_device,
        mesh=mesh,
        in_specs=(
            P("layer", "tok", None),
            P("layer", "tok", None),
            P("layer", "tok", None),
            P("layer", None),
            P("tok", None),
            P("layer", "tok", None),
        ),
        out_specs=(P("layer", "tok", None), P("layer", "tok", None)),
        check_vma=False,
    )
```

```python
import jax
import jax.numpy as jnp
from jax import lax
from jax.sharding import PartitionSpec as P

LANES = 128


def selectors(ids_all, range_size):
    base = lax.axis_index("tok") * range_size
    local = ids_all - base
    inside = (local >= 0) & (local < range_size)
    high = jnp.where(inside, local // LANES, -1)
    low = local % LANES
    high_hot = high[..., None] == jnp.arange(range_size // LANES, dtype=jnp.int32)
    low_hot = low[..., None] == jnp.arange(LANES, dtype=jnp.int32)
    return high_hot, low_hot


def exchange_codes(latent_ids, active_codes):
    owners = lax.axis_size("tok")
    top_count = latent_ids.shape[1]
    packed = jnp.concatenate(
        [latent_ids.astype(jnp.float32), active_codes.astype(jnp.float32)], axis=1
    )
    spread = jnp.broadcast_to(packed[None], (owners,) + packed.shape)
    gathered = lax.all_to_all(spread, "tok", split_axis=0, concat_axis=0, tiled=True)
    gathered = gathered.reshape(-1, 2 * top_count)
    ids_all = gathered[:, :top_count].astype(jnp.int32)
    codes_all = gathered[:, top_count:].astype(jnp.bfloat16)
    return ids_all, codes_all


def layer_chain(decoded, carry_gain, earlier_sum, targets):
    gains = lax.all_gather(carry_gain[0], "layer", axis=0, tiled=False)
    targets_all = lax.all_gather(targets[0], "layer", axis=0, tiled=False)
    decoded_all = lax.all_gather(decoded.astype(jnp.bfloat16), "layer", axis=0, tiled=False)
    layers = gains.shape[0]
    me = lax.axis_index("layer")
    carried = earlier_sum.astype(jnp.float32)
    misfits = []
    recon_own = jnp.zeros_like(decoded)
    for m in range(layers):
        own = me == m
        term = jnp.where(own, decoded, decoded_all[m].astype(jnp.float32))
        carried = term + gains[m][None, :] * carried
        recon_own = jnp.where(own, carried, recon_own)
        misfits.append(carried - targets_all[m].astype(jnp.float32))
    running = misfits[layers - 1]
    grad_own = jnp.where(me == layers - 1, running, jnp.zeros_like(running))
    for m in range(layers - 2, -1, -1):
        running = misfits[m] + gains[m + 1][None, :] * running
        grad_own = jnp.where(me == m, running, grad_own)
    return recon_own, grad_own


def on_device(active_codes, latent_ids, decoder, carry_gain, earlier_sum, targets):
    range_size = decoder.shape[1]
    owners = lax.axis_size("tok")
    weights = decoder[0]
    ids_all, codes_all = exchange_codes(latent_ids[0], active_codes[0])
    tokens = ids_all.shape[0]
    high_hot, low_hot = selectors(ids_all, range_size)
    coded_high = jnp.where(high_hot, codes_all[..., None], jnp.zeros((), jnp.bfloat16))
    spread = jnp.einsum(
        "tkh,tkl->thl", coded_high, low_hot.astype(jnp.bfloat16), preferred_element_type=jnp.float32
    )
    spread = spread.astype(jnp.bfloat16).reshape(tokens, range_size)
    partial = jnp.dot(spread, weights, preferred_element_type=jnp.float32).astype(jnp.bfloat16)
    decoded = lax.psum_scatter(partial, "tok", scatter_dimension=0, tiled=True).astype(jnp.float32)
    recon_full, grad_sum = layer_chain(decoded, carry_gain, earlier_sum, targets)
    grad_low = grad_sum.astype(jnp.bfloat16)
    segment = lax.all_gather(grad_low, "tok", axis=0, tiled=True)
    products = lax.dot_general(
        segment, weights, (((1,), (1,)), ((), ())), preferred_element_type=jnp.float32
    )
    products = products.reshape(tokens, range_size // LANES, LANES)
    picked_low = jnp.einsum(
        "thl,tkl->tkh",
        products,
        low_hot.astype(jnp.float32),
        precision=lax.Precision.HIGHEST,
        preferred_element_type=jnp.float32,
    )
    partial_grad = jnp.sum(jnp.where(high_hot, picked_low, 0.0), axis=-1)
    returned = lax.all_to_all(partial_grad, "tok", split_axis=0, concat_axis=0, tiled=True)
    code_grad = jnp.sum(returned.reshape(owners, -1, returned.shape[1]), axis=0)
    return (recon_full.astype(jnp.bfloat16)[None], code_grad[None])


def solution(mesh):
    return jax.shard_map(
        on_device,
        mesh=mesh,
        in_specs=(
            P("layer", "tok", None),
            P("layer", "tok", None),
            P("layer", "tok", None),
            P("layer", None),
            P("tok", None),
            P("layer", "tok", None),
        ),
        out_specs=(P("layer", "tok", None), P("layer", "tok", None)),
        check_vma=False,
    )
```

```python
import jax
import jax.numpy as jnp
from jax import lax
from jax.sharding import PartitionSpec as P

LANES = 128
CHUNKS = 4


def selectors(ids_all, range_size):
    base = lax.axis_index("tok") * range_size
    local = ids_all - base
    inside = (local >= 0) & (local < range_size)
    high = jnp.where(inside, local // LANES, -1)
    low = local % LANES
    high_hot = high[..., None] == jnp.arange(range_size // LANES, dtype=jnp.int32)
    low_hot = low[..., None] == jnp.arange(LANES, dtype=jnp.int32)
    return high_hot, low_hot


def exchange_codes(latent_ids, active_codes):
    owners = lax.axis_size("tok")
    top_count = latent_ids.shape[1]
    packed = jnp.concatenate(
        [latent_ids.astype(jnp.float32), active_codes.astype(jnp.float32)], axis=1
    )
    spread = jnp.broadcast_to(packed[None], (owners,) + packed.shape)
    gathered = lax.all_to_all(spread, "tok", split_axis=0, concat_axis=0, tiled=True)
    gathered = gathered.reshape(-1, 2 * top_count)
    ids_all = gathered[:, :top_count].astype(jnp.int32)
    codes_all = gathered[:, top_count:].astype(jnp.bfloat16)
    return ids_all, codes_all


def layer_chain(decoded, gains, earlier_sum, targets_all):
    decoded_all = lax.all_gather(decoded.astype(jnp.bfloat16), "layer", axis=0, tiled=False)
    layers = gains.shape[0]
    me = lax.axis_index("layer")
    carried = earlier_sum.astype(jnp.float32)
    misfits = []
    recon_own = jnp.zeros_like(decoded)
    for m in range(layers):
        own = me == m
        term = jnp.where(own, decoded, decoded_all[m].astype(jnp.float32))
        carried = term + gains[m][None, :] * carried
        recon_own = jnp.where(own, carried, recon_own)
        misfits.append(carried - targets_all[m].astype(jnp.float32))
    running = misfits[layers - 1]
    grad_own = jnp.where(me == layers - 1, running, jnp.zeros_like(running))
    for m in range(layers - 2, -1, -1):
        running = misfits[m] + gains[m + 1][None, :] * running
        grad_own = jnp.where(me == m, running, grad_own)
    return recon_own, grad_own


def on_device(active_codes, latent_ids, decoder, carry_gain, earlier_sum, targets):
    range_size = decoder.shape[1]
    owners = lax.axis_size("tok")
    weights = decoder[0]
    ids_all, codes_all = exchange_codes(latent_ids[0], active_codes[0])
    tokens = ids_all.shape[0]
    high_hot, low_hot = selectors(ids_all, range_size)
    coded_high = jnp.where(high_hot, codes_all[..., None], jnp.zeros((), jnp.bfloat16))
    spread = jnp.einsum(
        "tkh,tkl->thl", coded_high, low_hot.astype(jnp.bfloat16), preferred_element_type=jnp.float32
    )
    spread = spread.astype(jnp.bfloat16).reshape(tokens, range_size)
    width = weights.shape[1]
    pieces = CHUNKS if width % (CHUNKS * LANES) == 0 else 1
    step = width // pieces
    gains = lax.all_gather(carry_gain[0], "layer", axis=0, tiled=False)
    targets_all = lax.all_gather(targets[0], "layer", axis=0, tiled=False)
    recon_parts = []
    products = None
    for c in range(pieces):
        cols = slice(c * step, (c + 1) * step)
        w_part = weights[:, cols]
        partial = jnp.dot(spread, w_part, preferred_element_type=jnp.float32).astype(jnp.bfloat16)
        decoded = lax.psum_scatter(partial, "tok", scatter_dimension=0, tiled=True).astype(jnp.float32)
        recon_part, grad_part = layer_chain(
            decoded, gains[:, cols], earlier_sum[:, cols], targets_all[:, :, cols]
        )
        recon_parts.append(recon_part.astype(jnp.bfloat16))
        segment = lax.all_gather(grad_part.astype(jnp.bfloat16), "tok", axis=0, tiled=True)
        term = lax.dot_general(
            segment, w_part, (((1,), (1,)), ((), ())), preferred_element_type=jnp.float32
        )
        products = term if products is None else products + term
    recon_full = jnp.concatenate(recon_parts, axis=1)
    products = products.reshape(tokens, range_size // LANES, LANES)
    picked_low = jnp.einsum(
        "thl,tkl->tkh",
        products,
        low_hot.astype(jnp.float32),
        precision=lax.Precision.HIGHEST,
        preferred_element_type=jnp.float32,
    )
    partial_grad = jnp.sum(jnp.where(high_hot, picked_low, 0.0), axis=-1)
    returned = lax.all_to_all(partial_grad, "tok", split_axis=0, concat_axis=0, tiled=True)
    code_grad = jnp.sum(returned.reshape(owners, -1, returned.shape[1]), axis=0)
    return (recon_full[None], code_grad[None])


def solution(mesh):
    return jax.shard_map(
        on_device,
        mesh=mesh,
        in_specs=(
            P("layer", "tok", None),
            P("layer", "tok", None),
            P("layer", "tok", None),
            P("layer", None),
            P("tok", None),
            P("layer", "tok", None),
        ),
        out_specs=(P("layer", "tok", None), P("layer", "tok", None)),
        check_vma=False,
    )
```

```python
import functools

import jax
import jax.numpy as jnp
from jax import lax
from jax.sharding import PartitionSpec as P

LANES = 128


def selectors(ids_all, range_size):
    base = lax.axis_index("tok") * range_size
    local = ids_all - base
    inside = (local >= 0) & (local < range_size)
    high = jnp.where(inside, local // LANES, -1)
    low = local % LANES
    high_hot = high[..., None] == jnp.arange(range_size // LANES, dtype=jnp.int32)
    low_hot = low[..., None] == jnp.arange(LANES, dtype=jnp.int32)
    return high_hot, low_hot


def ring_order(mesh):
    count = mesh.shape["tok"]
    row = mesh.devices.reshape(-1, count)[0]
    coords = [getattr(device, "coords", None) for device in row]
    if any(c is None for c in coords):
        return list(range(count))
    varying = [d for d in range(len(coords[0])) if len({c[d] for c in coords}) > 1]
    if len(varying) != 2:
        return sorted(range(count), key=lambda i: tuple(coords[i]))
    sizes = [len({c[d] for c in coords}) for d in varying]
    outer, inner = (1, 0) if sizes[1] % 2 == 0 else (0, 1)
    place = {(coords[i][varying[outer]], coords[i][varying[inner]]): i for i in range(count)}
    outer_values = sorted({c[varying[outer]] for c in coords})
    inner_values = sorted({c[varying[inner]] for c in coords})
    order = []
    for n, o in enumerate(outer_values):
        walk = inner_values if n % 2 == 0 else inner_values[::-1]
        order.extend(place[(o, i)] for i in walk)
    return order


def ring_tables(ring):
    count = len(ring)
    position = [0] * count
    for p, i in enumerate(ring):
        position[i] = p
    forward = [(ring[p], ring[(p + 1) % count]) for p in range(count)]
    backward = [(ring[(p + 1) % count], ring[p]) for p in range(count)]
    here = jnp.asarray(position, jnp.int32)[lax.axis_index("tok")]
    return jnp.asarray(ring, jnp.int32), here, forward, backward


def ring_reduce_scatter(partial, ring):
    count = len(ring)
    members, here, forward, backward = ring_tables(ring)
    blocks = partial.reshape(count, -1, partial.shape[1])
    half = partial.shape[1] // 2
    sides = ((forward, -1, slice(0, half)), (backward, 1, slice(half, None)))
    results = []
    for perm, sign, cols in sides:
        own = blocks[:, :, cols]
        first = lax.dynamic_index_in_dim(own, members[(here + sign) % count], 0, keepdims=False)
        running = first
        for s in range(count - 1):
            arrived = lax.ppermute(running, "tok", perm)
            block = members[(here + sign * (s + 2)) % count]
            total = arrived.astype(jnp.float32) + lax.dynamic_index_in_dim(
                own, block, 0, keepdims=False
            ).astype(jnp.float32)
            running = total.astype(jnp.bfloat16)
        results.append(total)
    return jnp.concatenate(results, axis=1)


def ring_all_gather(piece, ring):
    count = len(ring)
    members, here, forward, backward = ring_tables(ring)
    half = piece.shape[1] // 2
    gathered = jnp.zeros((count,) + piece.shape, piece.dtype)
    me = lax.axis_index("tok")
    gathered = lax.dynamic_update_index_in_dim(gathered, piece, me, 0)
    sides = ((forward, -1, 0, piece[:, :half]), (backward, 1, half, piece[:, half:]))
    for perm, sign, offset, travelling in sides:
        for s in range(count - 1):
            travelling = lax.ppermute(travelling, "tok", perm)
            source = members[(here + sign * (s + 1)) % count]
            gathered = lax.dynamic_update_slice(
                gathered, travelling[None], (source, jnp.int32(0), jnp.int32(offset))
            )
    return gathered.reshape(count * piece.shape[0], piece.shape[1])


def exchange_codes(latent_ids, active_codes):
    owners = lax.axis_size("tok")
    top_count = latent_ids.shape[1]
    packed = jnp.concatenate(
        [latent_ids.astype(jnp.float32), active_codes.astype(jnp.float32)], axis=1
    )
    spread = jnp.broadcast_to(packed[None], (owners,) + packed.shape)
    gathered = lax.all_to_all(spread, "tok", split_axis=0, concat_axis=0, tiled=True)
    gathered = gathered.reshape(-1, 2 * top_count)
    ids_all = gathered[:, :top_count].astype(jnp.int32)
    codes_all = gathered[:, top_count:].astype(jnp.bfloat16)
    return ids_all, codes_all


def layer_chain(decoded, carry_gain, earlier_sum, targets):
    gains = lax.all_gather(carry_gain[0], "layer", axis=0, tiled=False)
    targets_all = lax.all_gather(targets[0], "layer", axis=0, tiled=False)
    decoded_all = lax.all_gather(decoded.astype(jnp.bfloat16), "layer", axis=0, tiled=False)
    layers = gains.shape[0]
    me = lax.axis_index("layer")
    carried = earlier_sum.astype(jnp.float32)
    misfits = []
    recon_own = jnp.zeros_like(decoded)
    for m in range(layers):
        own = me == m
        term = jnp.where(own, decoded, decoded_all[m].astype(jnp.float32))
        carried = term + gains[m][None, :] * carried
        recon_own = jnp.where(own, carried, recon_own)
        misfits.append(carried - targets_all[m].astype(jnp.float32))
    running = misfits[layers - 1]
    grad_own = jnp.where(me == layers - 1, running, jnp.zeros_like(running))
    for m in range(layers - 2, -1, -1):
        running = misfits[m] + gains[m + 1][None, :] * running
        grad_own = jnp.where(me == m, running, grad_own)
    return recon_own, grad_own


def on_device(ring, active_codes, latent_ids, decoder, carry_gain, earlier_sum, targets):
    range_size = decoder.shape[1]
    owners = lax.axis_size("tok")
    weights = decoder[0]
    ids_all, codes_all = exchange_codes(latent_ids[0], active_codes[0])
    tokens = ids_all.shape[0]
    high_hot, low_hot = selectors(ids_all, range_size)
    coded_high = jnp.where(high_hot, codes_all[..., None], jnp.zeros((), jnp.bfloat16))
    spread = jnp.einsum(
        "tkh,tkl->thl", coded_high, low_hot.astype(jnp.bfloat16), preferred_element_type=jnp.float32
    )
    spread = spread.astype(jnp.bfloat16).reshape(tokens, range_size)
    partial = jnp.dot(spread, weights, preferred_element_type=jnp.float32).astype(jnp.bfloat16)
    decoded = ring_reduce_scatter(partial, ring)
    recon_full, grad_sum = layer_chain(decoded, carry_gain, earlier_sum, targets)
    grad_low = grad_sum.astype(jnp.bfloat16)
    segment = ring_all_gather(grad_low, ring)
    products = lax.dot_general(
        segment, weights, (((1,), (1,)), ((), ())), preferred_element_type=jnp.float32
    )
    products = products.reshape(tokens, range_size // LANES, LANES)
    picked_low = jnp.einsum(
        "thl,tkl->tkh",
        products,
        low_hot.astype(jnp.float32),
        precision=lax.Precision.HIGHEST,
        preferred_element_type=jnp.float32,
    )
    partial_grad = jnp.sum(jnp.where(high_hot, picked_low, 0.0), axis=-1)
    returned = lax.all_to_all(partial_grad, "tok", split_axis=0, concat_axis=0, tiled=True)
    code_grad = jnp.sum(returned.reshape(owners, -1, returned.shape[1]), axis=0)
    return (recon_full.astype(jnp.bfloat16)[None], code_grad[None])


def solution(mesh):
    ring = ring_order(mesh)
    return jax.shard_map(
        functools.partial(on_device, ring),
        mesh=mesh,
        in_specs=(
            P("layer", "tok", None),
            P("layer", "tok", None),
            P("layer", "tok", None),
            P("layer", None),
            P("tok", None),
            P("layer", "tok", None),
        ),
        out_specs=(P("layer", "tok", None), P("layer", "tok", None)),
        check_vma=False,
    )
```

```python
import jax
import jax.numpy as jnp
from jax import lax
from jax.sharding import PartitionSpec as P

LANES = 128


def selectors(ids_all, range_size):
    base = lax.axis_index("tok") * range_size
    local = ids_all - base
    inside = (local >= 0) & (local < range_size)
    high = jnp.where(inside, local // LANES, -1)
    low = local % LANES
    high_hot = high[..., None] == jnp.arange(range_size // LANES, dtype=jnp.int32)
    low_hot = low[..., None] == jnp.arange(LANES, dtype=jnp.int32)
    return high_hot, low_hot


def exchange_codes(latent_ids, active_codes):
    owners = lax.axis_size("tok")
    top_count = latent_ids.shape[1]
    packed = jnp.concatenate(
        [latent_ids.astype(jnp.float32), active_codes.astype(jnp.float32)], axis=1
    )
    spread = jnp.broadcast_to(packed[None], (owners,) + packed.shape)
    gathered = lax.all_to_all(spread, "tok", split_axis=0, concat_axis=0, tiled=True)
    gathered = gathered.reshape(-1, 2 * top_count)
    ids_all = gathered[:, :top_count].astype(jnp.int32)
    codes_all = gathered[:, top_count:].astype(jnp.bfloat16)
    return ids_all, codes_all


def layer_chain(decoded, carry_gain, earlier_sum, targets):
    gains = lax.all_gather(carry_gain[0], "layer", axis=0, tiled=False)
    targets_all = lax.all_gather(targets[0], "layer", axis=0, tiled=False)
    decoded_all = lax.all_gather(decoded.astype(jnp.bfloat16), "layer", axis=0, tiled=False)
    layers = gains.shape[0]
    me = lax.axis_index("layer")
    carried = earlier_sum.astype(jnp.float32)
    misfits = []
    recon_own = jnp.zeros_like(decoded)
    for m in range(layers):
        own = me == m
        term = jnp.where(own, decoded, decoded_all[m].astype(jnp.float32))
        carried = term + gains[m][None, :] * carried
        recon_own = jnp.where(own, carried, recon_own)
        misfits.append(carried - targets_all[m].astype(jnp.float32))
    running = misfits[layers - 1]
    grad_own = jnp.where(me == layers - 1, running, jnp.zeros_like(running))
    for m in range(layers - 2, -1, -1):
        running = misfits[m] + gains[m + 1][None, :] * running
        grad_own = jnp.where(me == m, running, grad_own)
    return recon_own, grad_own


def on_device(active_codes, latent_ids, decoder, carry_gain, earlier_sum, targets):
    range_size = decoder.shape[1]
    owners = lax.axis_size("tok")
    weights = decoder[0]
    ids_all, codes_all = exchange_codes(latent_ids[0], active_codes[0])
    tokens = ids_all.shape[0]
    high_hot, low_hot = selectors(ids_all, range_size)
    coded_high = jnp.where(high_hot, codes_all[..., None], jnp.zeros((), jnp.bfloat16))
    spread = jnp.einsum(
        "tkh,tkl->thl", coded_high, low_hot.astype(jnp.bfloat16), preferred_element_type=jnp.float32
    )
    spread = spread.astype(jnp.bfloat16).reshape(tokens, range_size)
    partial = jnp.dot(spread, weights, preferred_element_type=jnp.float32).astype(jnp.bfloat16)
    received = lax.all_to_all(partial, "tok", split_axis=0, concat_axis=0, tiled=True)
    decoded = jnp.sum(
        received.reshape(owners, -1, received.shape[1]).astype(jnp.float32), axis=0
    )
    recon_full, grad_sum = layer_chain(decoded, carry_gain, earlier_sum, targets)
    grad_low = grad_sum.astype(jnp.bfloat16)
    copies = jnp.broadcast_to(grad_low[None], (owners,) + grad_low.shape)
    segment = lax.all_to_all(copies, "tok", split_axis=0, concat_axis=0, tiled=True)
    segment = segment.reshape(owners * grad_low.shape[0], grad_low.shape[1])
    products = lax.dot_general(
        segment, weights, (((1,), (1,)), ((), ())), preferred_element_type=jnp.float32
    )
    products = products.reshape(tokens, range_size // LANES, LANES)
    picked_low = jnp.einsum(
        "thl,tkl->tkh",
        products,
        low_hot.astype(jnp.float32),
        precision=lax.Precision.HIGHEST,
        preferred_element_type=jnp.float32,
    )
    partial_grad = jnp.sum(jnp.where(high_hot, picked_low, 0.0), axis=-1)
    returned = lax.all_to_all(partial_grad, "tok", split_axis=0, concat_axis=0, tiled=True)
    code_grad = jnp.sum(returned.reshape(owners, -1, returned.shape[1]), axis=0)
    return (recon_full.astype(jnp.bfloat16)[None], code_grad[None])


def solution(mesh):
    return jax.shard_map(
        on_device,
        mesh=mesh,
        in_specs=(
            P("layer", "tok", None),
            P("layer", "tok", None),
            P("layer", "tok", None),
            P("layer", None),
            P("tok", None),
            P("layer", "tok", None),
        ),
        out_specs=(P("layer", "tok", None), P("layer", "tok", None)),
        check_vma=False,
    )
```

```python
import jax
import jax.numpy as jnp
from jax import lax
from jax.sharding import PartitionSpec as P

LANES = 128


def selectors(ids_all, range_size):
    base = lax.axis_index("tok") * range_size
    local = ids_all - base
    inside = (local >= 0) & (local < range_size)
    high = jnp.where(inside, local // LANES, -1)
    low = local % LANES
    high_hot = high[..., None] == jnp.arange(range_size // LANES, dtype=jnp.int32)
    low_hot = low[..., None] == jnp.arange(LANES, dtype=jnp.int32)
    return high_hot, low_hot


def exchange_codes(latent_ids, active_codes):
    owners = lax.axis_size("tok")
    top_count = latent_ids.shape[1]
    packed = jnp.concatenate(
        [latent_ids.astype(jnp.float32), active_codes.astype(jnp.float32)], axis=1
    )
    spread = jnp.broadcast_to(packed[None], (owners,) + packed.shape)
    gathered = lax.all_to_all(spread, "tok", split_axis=0, concat_axis=0, tiled=True)
    gathered = gathered.reshape(-1, 2 * top_count)
    ids_all = gathered[:, :top_count].astype(jnp.int32)
    codes_all = gathered[:, top_count:].astype(jnp.bfloat16)
    return ids_all, codes_all


def layer_chain(decoded, carry_gain, earlier_sum, targets):
    gains = lax.all_gather(carry_gain[0], "layer", axis=0, tiled=False)
    targets_all = lax.all_gather(targets[0], "layer", axis=0, tiled=False)
    decoded_all = lax.all_gather(decoded.astype(jnp.bfloat16), "layer", axis=0, tiled=False)
    layers = gains.shape[0]
    me = lax.axis_index("layer")
    carried = earlier_sum.astype(jnp.float32)
    misfits = []
    recon_own = jnp.zeros_like(decoded)
    for m in range(layers):
        own = me == m
        term = jnp.where(own, decoded, decoded_all[m].astype(jnp.float32))
        carried = term + gains[m][None, :] * carried
        recon_own = jnp.where(own, carried, recon_own)
        misfits.append(carried - targets_all[m].astype(jnp.float32))
    running = misfits[layers - 1]
    grad_own = jnp.where(me == layers - 1, running, jnp.zeros_like(running))
    for m in range(layers - 2, -1, -1):
        running = misfits[m] + gains[m + 1][None, :] * running
        grad_own = jnp.where(me == m, running, grad_own)
    return recon_own, grad_own


def on_device(active_codes, latent_ids, decoder, carry_gain, earlier_sum, targets):
    range_size = decoder.shape[1]
    owners = lax.axis_size("tok")
    weights = decoder[0]
    ids_all, codes_all = exchange_codes(latent_ids[0], active_codes[0])
    tokens = ids_all.shape[0]
    high_hot, low_hot = selectors(ids_all, range_size)
    coded_high = jnp.where(high_hot, codes_all[..., None], jnp.zeros((), jnp.bfloat16))
    spread = jnp.einsum(
        "tkh,tkl->thl", coded_high, low_hot.astype(jnp.bfloat16), preferred_element_type=jnp.float32
    )
    spread = spread.astype(jnp.bfloat16).reshape(tokens, range_size)
    half = weights.shape[1] // 2
    w_first, w_second = weights[:, :half], weights[:, half:]
    partial_first = jnp.dot(spread, w_first, preferred_element_type=jnp.float32).astype(jnp.bfloat16)
    decoded_first = lax.psum_scatter(partial_first, "tok", scatter_dimension=0, tiled=True)
    partial_second = jnp.dot(spread, w_second, preferred_element_type=jnp.float32).astype(jnp.bfloat16)
    received = lax.all_to_all(partial_second, "tok", split_axis=0, concat_axis=0, tiled=True)
    decoded_second = jnp.sum(
        received.reshape(owners, -1, received.shape[1]).astype(jnp.float32), axis=0
    )
    decoded = jnp.concatenate([decoded_first.astype(jnp.float32), decoded_second], axis=1)
    recon_full, grad_sum = layer_chain(decoded, carry_gain, earlier_sum, targets)
    grad_low = grad_sum.astype(jnp.bfloat16)
    segment_first = lax.all_gather(grad_low[:, :half], "tok", axis=0, tiled=True)
    copies = jnp.broadcast_to(grad_low[None, :, half:], (owners, grad_low.shape[0], half))
    segment_second = lax.all_to_all(copies, "tok", split_axis=0, concat_axis=0, tiled=True)
    segment = jnp.concatenate(
        [segment_first, segment_second.reshape(owners * grad_low.shape[0], half)], axis=1
    )
    products = lax.dot_general(
        segment, weights, (((1,), (1,)), ((), ())), preferred_element_type=jnp.float32
    )
    products = products.reshape(tokens, range_size // LANES, LANES)
    picked_low = jnp.einsum(
        "thl,tkl->tkh",
        products,
        low_hot.astype(jnp.float32),
        precision=lax.Precision.HIGHEST,
        preferred_element_type=jnp.float32,
    )
    partial_grad = jnp.sum(jnp.where(high_hot, picked_low, 0.0), axis=-1)
    returned = lax.all_to_all(partial_grad, "tok", split_axis=0, concat_axis=0, tiled=True)
    code_grad = jnp.sum(returned.reshape(owners, -1, returned.shape[1]), axis=0)
    return (recon_full.astype(jnp.bfloat16)[None], code_grad[None])


def solution(mesh):
    return jax.shard_map(
        on_device,
        mesh=mesh,
        in_specs=(
            P("layer", "tok", None),
            P("layer", "tok", None),
            P("layer", "tok", None),
            P("layer", None),
            P("tok", None),
            P("layer", "tok", None),
        ),
        out_specs=(P("layer", "tok", None), P("layer", "tok", None)),
        check_vma=False,
    )
```

```python
import jax
import jax.numpy as jnp
from jax import lax
from jax.sharding import PartitionSpec as P

LANES = 128


def selectors(ids_all, range_size):
    base = lax.axis_index("tok") * range_size
    local = ids_all - base
    inside = (local >= 0) & (local < range_size)
    high = jnp.where(inside, local // LANES, -1)
    low = local % LANES
    high_hot = high[..., None] == jnp.arange(range_size // LANES, dtype=jnp.int32)
    low_hot = low[..., None] == jnp.arange(LANES, dtype=jnp.int32)
    return high_hot, low_hot


def exchange_codes(latent_ids, active_codes):
    owners = lax.axis_size("tok")
    top_count = latent_ids.shape[1]
    packed = jnp.concatenate(
        [latent_ids.astype(jnp.float32), active_codes.astype(jnp.float32)], axis=1
    )
    spread = jnp.broadcast_to(packed[None], (owners,) + packed.shape)
    gathered = lax.all_to_all(spread, "tok", split_axis=0, concat_axis=0, tiled=True)
    gathered = gathered.reshape(-1, 2 * top_count)
    ids_all = gathered[:, :top_count].astype(jnp.int32)
    codes_all = gathered[:, top_count:].astype(jnp.bfloat16)
    return ids_all, codes_all


def layer_chain(decoded, carry_gain, earlier_sum, targets):
    gains = lax.all_gather(carry_gain[0], "layer", axis=0, tiled=False)
    targets_all = lax.all_gather(targets[0], "layer", axis=0, tiled=False)
    decoded_all = lax.all_gather(decoded.astype(jnp.bfloat16), "layer", axis=0, tiled=False)
    layers = gains.shape[0]
    me = lax.axis_index("layer")
    carried = earlier_sum.astype(jnp.float32)
    misfits = []
    recon_own = jnp.zeros_like(decoded)
    for m in range(layers):
        own = me == m
        term = jnp.where(own, decoded, decoded_all[m].astype(jnp.float32))
        carried = term + gains[m][None, :] * carried
        recon_own = jnp.where(own, carried, recon_own)
        misfits.append(carried - targets_all[m].astype(jnp.float32))
    running = misfits[layers - 1]
    grad_own = jnp.where(me == layers - 1, running, jnp.zeros_like(running))
    for m in range(layers - 2, -1, -1):
        running = misfits[m] + gains[m + 1][None, :] * running
        grad_own = jnp.where(me == m, running, grad_own)
    return recon_own, grad_own


def on_device(active_codes, latent_ids, decoder, carry_gain, earlier_sum, targets):
    range_size = decoder.shape[1]
    owners = lax.axis_size("tok")
    weights = decoder[0]
    ids_all, codes_all = exchange_codes(latent_ids[0], active_codes[0])
    tokens = ids_all.shape[0]
    high_hot, low_hot = selectors(ids_all, range_size)
    coded_high = jnp.where(high_hot, codes_all[..., None], jnp.zeros((), jnp.bfloat16))
    spread = jnp.einsum(
        "tkh,tkl->thl", coded_high, low_hot.astype(jnp.bfloat16), preferred_element_type=jnp.float32
    )
    spread = spread.astype(jnp.bfloat16).reshape(tokens, range_size)
    half = weights.shape[1] // 2
    w_first, w_second = weights[:, :half], weights[:, half:]
    partial_first = jnp.dot(spread, w_first, preferred_element_type=jnp.float32).astype(jnp.bfloat16)
    decoded_first = lax.psum_scatter(partial_first, "tok", scatter_dimension=0, tiled=True)
    partial_second = jnp.dot(spread, w_second, preferred_element_type=jnp.float32).astype(jnp.bfloat16)
    received = lax.all_to_all(partial_second, "tok", split_axis=0, concat_axis=0, tiled=True)
    decoded_second = jnp.sum(
        received.reshape(owners, -1, received.shape[1]).astype(jnp.float32), axis=0
    )
    decoded = jnp.concatenate([decoded_first.astype(jnp.float32), decoded_second], axis=1)
    recon_full, grad_sum = layer_chain(decoded, carry_gain, earlier_sum, targets)
    grad_low = grad_sum.astype(jnp.bfloat16)
    segment = lax.all_gather(grad_low, "tok", axis=0, tiled=True)
    products = lax.dot_general(
        segment, weights, (((1,), (1,)), ((), ())), preferred_element_type=jnp.float32
    )
    products = products.reshape(tokens, range_size // LANES, LANES)
    picked_low = jnp.einsum(
        "thl,tkl->tkh",
        products,
        low_hot.astype(jnp.float32),
        precision=lax.Precision.HIGH,
        preferred_element_type=jnp.float32,
    )
    partial_grad = jnp.sum(jnp.where(high_hot, picked_low, 0.0), axis=-1)
    returned = lax.all_to_all(partial_grad, "tok", split_axis=0, concat_axis=0, tiled=True)
    code_grad = jnp.sum(returned.reshape(owners, -1, returned.shape[1]), axis=0)
    return (recon_full.astype(jnp.bfloat16)[None], code_grad[None])


def solution(mesh):
    return jax.shard_map(
        on_device,
        mesh=mesh,
        in_specs=(
            P("layer", "tok", None),
            P("layer", "tok", None),
            P("layer", "tok", None),
            P("layer", None),
            P("tok", None),
            P("layer", "tok", None),
        ),
        out_specs=(P("layer", "tok", None), P("layer", "tok", None)),
        check_vma=False,
    )
```

```python
import jax
import jax.numpy as jnp
from jax import lax
from jax.sharding import PartitionSpec as P

LANES = 128


def selectors(ids_all, range_size):
    base = lax.axis_index("tok") * range_size
    local = ids_all - base
    inside = (local >= 0) & (local < range_size)
    high = jnp.where(inside, local // LANES, -1)
    low = local % LANES
    high_hot = high[..., None] == jnp.arange(range_size // LANES, dtype=jnp.int32)
    low_hot = low[..., None] == jnp.arange(LANES, dtype=jnp.int32)
    return high_hot, low_hot


def exchange_codes(latent_ids, active_codes):
    owners = lax.axis_size("tok")
    top_count = latent_ids.shape[1]
    packed = jnp.concatenate(
        [latent_ids.astype(jnp.float32), active_codes.astype(jnp.float32)], axis=1
    )
    spread = jnp.broadcast_to(packed[None], (owners,) + packed.shape)
    gathered = lax.all_to_all(spread, "tok", split_axis=0, concat_axis=0, tiled=True)
    gathered = gathered.reshape(-1, 2 * top_count)
    ids_all = gathered[:, :top_count].astype(jnp.int32)
    codes_all = gathered[:, top_count:].astype(jnp.bfloat16)
    return ids_all, codes_all


def layer_chain(decoded, carry_gain, earlier_sum, targets):
    gain = carry_gain[0][None, :]
    gain_high = gain.astype(jnp.bfloat16)
    rest = gain - gain_high.astype(jnp.float32)
    gain_mid = rest.astype(jnp.bfloat16)
    gain_low = (rest - gain_mid.astype(jnp.float32)).astype(jnp.bfloat16)
    rows = targets.shape[1]
    packed = jnp.concatenate([targets[0], gain_high, gain_mid, gain_low], axis=0)
    packed_all = lax.all_gather(packed, "layer", axis=0, tiled=False)
    targets_all = packed_all[:, :rows]
    gains = (
        packed_all[:, rows].astype(jnp.float32)
        + packed_all[:, rows + 1].astype(jnp.float32)
        + packed_all[:, rows + 2].astype(jnp.float32)
    )
    decoded_all = lax.all_gather(decoded.astype(jnp.bfloat16), "layer", axis=0, tiled=False)
    layers = gains.shape[0]
    me = lax.axis_index("layer")
    carried = earlier_sum.astype(jnp.float32)
    misfits = []
    recon_own = jnp.zeros_like(decoded)
    for m in range(layers):
        own = me == m
        term = jnp.where(own, decoded, decoded_all[m].astype(jnp.float32))
        carried = term + gains[m][None, :] * carried
        recon_own = jnp.where(own, carried, recon_own)
        misfits.append(carried - targets_all[m].astype(jnp.float32))
    running = misfits[layers - 1]
    grad_own = jnp.where(me == layers - 1, running, jnp.zeros_like(running))
    for m in range(layers - 2, -1, -1):
        running = misfits[m] + gains[m + 1][None, :] * running
        grad_own = jnp.where(me == m, running, grad_own)
    return recon_own, grad_own


def on_device(active_codes, latent_ids, decoder, carry_gain, earlier_sum, targets):
    range_size = decoder.shape[1]
    owners = lax.axis_size("tok")
    weights = decoder[0]
    ids_all, codes_all = exchange_codes(latent_ids[0], active_codes[0])
    tokens = ids_all.shape[0]
    high_hot, low_hot = selectors(ids_all, range_size)
    coded_high = jnp.where(high_hot, codes_all[..., None], jnp.zeros((), jnp.bfloat16))
    spread = jnp.einsum(
        "tkh,tkl->thl", coded_high, low_hot.astype(jnp.bfloat16), preferred_element_type=jnp.float32
    )
    spread = spread.astype(jnp.bfloat16).reshape(tokens, range_size)
    half = weights.shape[1] // 2
    w_first, w_second = weights[:, :half], weights[:, half:]
    partial_first = jnp.dot(spread, w_first, preferred_element_type=jnp.float32).astype(jnp.bfloat16)
    decoded_first = lax.psum_scatter(partial_first, "tok", scatter_dimension=0, tiled=True)
    partial_second = jnp.dot(spread, w_second, preferred_element_type=jnp.float32).astype(jnp.bfloat16)
    received = lax.all_to_all(partial_second, "tok", split_axis=0, concat_axis=0, tiled=True)
    decoded_second = jnp.sum(
        received.reshape(owners, -1, received.shape[1]).astype(jnp.float32), axis=0
    )
    decoded = jnp.concatenate([decoded_first.astype(jnp.float32), decoded_second], axis=1)
    recon_full, grad_sum = layer_chain(decoded, carry_gain, earlier_sum, targets)
    grad_low = grad_sum.astype(jnp.bfloat16)
    rows = grad_low.shape[0]
    pieces = 2 if rows % 32 == 0 else 1
    span = rows // pieces
    picked = []
    for c in range(pieces):
        segment = lax.all_gather(grad_low[c * span:(c + 1) * span], "tok", axis=0, tiled=True)
        products = lax.dot_general(
            segment, weights, (((1,), (1,)), ((), ())), preferred_element_type=jnp.float32
        )
        products = products.reshape(owners * span, range_size // LANES, LANES)
        own_rows = lambda a: a.reshape((owners, rows) + a.shape[1:])[:, c * span:(c + 1) * span].reshape(
            (owners * span,) + a.shape[1:]
        )
        picked_low = jnp.einsum(
            "thl,tkl->tkh",
            products,
            own_rows(low_hot).astype(jnp.float32),
            precision=lax.Precision.HIGH,
            preferred_element_type=jnp.float32,
        )
        chosen = jnp.sum(jnp.where(own_rows(high_hot), picked_low, 0.0), axis=-1)
        picked.append(chosen.reshape(owners, span, -1))
    partial_grad = jnp.concatenate(picked, axis=1).reshape(owners * rows, -1)
    returned = lax.all_to_all(partial_grad, "tok", split_axis=0, concat_axis=0, tiled=True)
    code_grad = jnp.sum(returned.reshape(owners, -1, returned.shape[1]), axis=0)
    return (recon_full.astype(jnp.bfloat16)[None], code_grad[None])


def solution(mesh):
    return jax.shard_map(
        on_device,
        mesh=mesh,
        in_specs=(
            P("layer", "tok", None),
            P("layer", "tok", None),
            P("layer", "tok", None),
            P("layer", None),
            P("tok", None),
            P("layer", "tok", None),
        ),
        out_specs=(P("layer", "tok", None), P("layer", "tok", None)),
        check_vma=False,
    )
```

```python
import jax
import jax.numpy as jnp
from jax import lax
from jax.sharding import PartitionSpec as P

LANES = 128


def selectors(ids_all, range_size):
    base = lax.axis_index("tok") * range_size
    local = ids_all - base
    inside = (local >= 0) & (local < range_size)
    high = jnp.where(inside, local // LANES, -1)
    low = local % LANES
    high_hot = high[..., None] == jnp.arange(range_size // LANES, dtype=jnp.int32)
    low_hot = low[..., None] == jnp.arange(LANES, dtype=jnp.int32)
    return high_hot, low_hot


def exchange_codes(latent_ids, active_codes):
    owners = lax.axis_size("tok")
    top_count = latent_ids.shape[1]
    packed = jnp.concatenate(
        [latent_ids.astype(jnp.float32), active_codes.astype(jnp.float32)], axis=1
    )
    spread = jnp.broadcast_to(packed[None], (owners,) + packed.shape)
    gathered = lax.all_to_all(spread, "tok", split_axis=0, concat_axis=0, tiled=True)
    gathered = gathered.reshape(-1, 2 * top_count)
    ids_all = gathered[:, :top_count].astype(jnp.int32)
    codes_all = gathered[:, top_count:].astype(jnp.bfloat16)
    return ids_all, codes_all


def layer_chain(decoded, carry_gain, earlier_sum, targets):
    gains = lax.all_gather(carry_gain[0], "layer", axis=0, tiled=False)
    targets_all = lax.all_gather(targets[0], "layer", axis=0, tiled=False)
    decoded_all = lax.all_gather(decoded.astype(jnp.bfloat16), "layer", axis=0, tiled=False)
    layers = gains.shape[0]
    me = lax.axis_index("layer")
    carried = earlier_sum.astype(jnp.float32)
    misfits = []
    recon_own = jnp.zeros_like(decoded)
    for m in range(layers):
        own = me == m
        term = jnp.where(own, decoded, decoded_all[m].astype(jnp.float32))
        carried = term + gains[m][None, :] * carried
        recon_own = jnp.where(own, carried, recon_own)
        misfits.append(carried - targets_all[m].astype(jnp.float32))
    running = misfits[layers - 1]
    grad_own = jnp.where(me == layers - 1, running, jnp.zeros_like(running))
    for m in range(layers - 2, -1, -1):
        running = misfits[m] + gains[m + 1][None, :] * running
        grad_own = jnp.where(me == m, running, grad_own)
    return recon_own, grad_own


def on_device(active_codes, latent_ids, decoder, carry_gain, earlier_sum, targets):
    range_size = decoder.shape[1]
    owners = lax.axis_size("tok")
    weights = decoder[0]
    ids_all, codes_all = exchange_codes(latent_ids[0], active_codes[0])
    tokens = ids_all.shape[0]
    high_hot, low_hot = selectors(ids_all, range_size)
    coded_high = jnp.where(high_hot, codes_all[..., None], jnp.zeros((), jnp.bfloat16))
    spread = jnp.einsum(
        "tkh,tkl->thl", coded_high, low_hot.astype(jnp.bfloat16), preferred_element_type=jnp.float32
    )
    spread = spread.astype(jnp.bfloat16).reshape(tokens, range_size)
    half = weights.shape[1] // 4 if weights.shape[1] % (4 * LANES) == 0 else weights.shape[1] // 2
    w_first, w_second = weights[:, :half], weights[:, half:]
    partial_first = jnp.dot(spread, w_first, preferred_element_type=jnp.float32).astype(jnp.bfloat16)
    decoded_first = lax.psum_scatter(partial_first, "tok", scatter_dimension=0, tiled=True)
    partial_second = jnp.dot(spread, w_second, preferred_element_type=jnp.float32).astype(jnp.bfloat16)
    received = lax.all_to_all(partial_second, "tok", split_axis=0, concat_axis=0, tiled=True)
    decoded_second = jnp.sum(
        received.reshape(owners, -1, received.shape[1]).astype(jnp.float32), axis=0
    )
    decoded = jnp.concatenate([decoded_first.astype(jnp.float32), decoded_second], axis=1)
    recon_full, grad_sum = layer_chain(decoded, carry_gain, earlier_sum, targets)
    grad_low = grad_sum.astype(jnp.bfloat16)
    segment = lax.all_gather(grad_low, "tok", axis=0, tiled=True)
    products = lax.dot_general(
        segment, weights, (((1,), (1,)), ((), ())), preferred_element_type=jnp.float32
    )
    products = products.reshape(tokens, range_size // LANES, LANES)
    products_high = products.astype(jnp.bfloat16)
    products_low = (products - products_high.astype(jnp.float32)).astype(jnp.bfloat16)
    low_pick = low_hot.astype(jnp.bfloat16)
    picked_low = jnp.einsum(
        "thl,tkl->tkh", products_high, low_pick, preferred_element_type=jnp.float32
    ) + jnp.einsum("thl,tkl->tkh", products_low, low_pick, preferred_element_type=jnp.float32)
    partial_grad = jnp.sum(jnp.where(high_hot, picked_low, 0.0), axis=-1)
    returned = lax.all_to_all(partial_grad, "tok", split_axis=0, concat_axis=0, tiled=True)
    code_grad = jnp.sum(returned.reshape(owners, -1, returned.shape[1]), axis=0)
    return (recon_full.astype(jnp.bfloat16)[None], code_grad[None])


def solution(mesh):
    return jax.shard_map(
        on_device,
        mesh=mesh,
        in_specs=(
            P("layer", "tok", None),
            P("layer", "tok", None),
            P("layer", "tok", None),
            P("layer", None),
            P("tok", None),
            P("layer", "tok", None),
        ),
        out_specs=(P("layer", "tok", None), P("layer", "tok", None)),
        check_vma=False,
    )
```

```python
import jax
import jax.numpy as jnp
from jax import lax
from jax.sharding import PartitionSpec as P

LANES = 128


def selectors(ids_all, range_size):
    base = lax.axis_index("tok") * range_size
    local = ids_all - base
    inside = (local >= 0) & (local < range_size)
    high = jnp.where(inside, local // LANES, -1)
    low = local % LANES
    high_hot = high[..., None] == jnp.arange(range_size // LANES, dtype=jnp.int32)
    low_hot = low[..., None] == jnp.arange(LANES, dtype=jnp.int32)
    return high_hot, low_hot


def exchange_codes(latent_ids, active_codes):
    owners = lax.axis_size("tok")
    top_count = latent_ids.shape[1]
    packed = jnp.concatenate(
        [latent_ids.astype(jnp.float32), active_codes.astype(jnp.float32)], axis=1
    )
    spread = jnp.broadcast_to(packed[None], (owners,) + packed.shape)
    gathered = lax.all_to_all(spread, "tok", split_axis=0, concat_axis=0, tiled=True)
    gathered = gathered.reshape(-1, 2 * top_count)
    ids_all = gathered[:, :top_count].astype(jnp.int32)
    codes_all = gathered[:, top_count:].astype(jnp.bfloat16)
    return ids_all, codes_all


def layer_chain(decoded, carry_gain, earlier_sum, targets):
    gains = lax.all_gather(carry_gain[0], "layer", axis=0, tiled=False)
    targets_all = lax.all_gather(targets[0], "layer", axis=0, tiled=False)
    decoded_all = lax.all_gather(decoded.astype(jnp.bfloat16), "layer", axis=0, tiled=False)
    layers = gains.shape[0]
    me = lax.axis_index("layer")
    carried = earlier_sum.astype(jnp.float32)
    misfits = []
    recon_own = jnp.zeros_like(decoded)
    for m in range(layers):
        own = me == m
        term = jnp.where(own, decoded, decoded_all[m].astype(jnp.float32))
        carried = term + gains[m][None, :] * carried
        recon_own = jnp.where(own, carried, recon_own)
        misfits.append(carried - targets_all[m].astype(jnp.float32))
    running = misfits[layers - 1]
    grad_own = jnp.where(me == layers - 1, running, jnp.zeros_like(running))
    for m in range(layers - 2, -1, -1):
        running = misfits[m] + gains[m + 1][None, :] * running
        grad_own = jnp.where(me == m, running, grad_own)
    return recon_own, grad_own


def on_device(active_codes, latent_ids, decoder, carry_gain, earlier_sum, targets):
    range_size = decoder.shape[1]
    owners = lax.axis_size("tok")
    weights = decoder[0]
    ids_all, codes_all = exchange_codes(latent_ids[0], active_codes[0])
    tokens = ids_all.shape[0]
    high_hot, low_hot = selectors(ids_all, range_size)
    coded_high = jnp.where(high_hot, codes_all[..., None], jnp.zeros((), jnp.bfloat16))
    spread = jnp.einsum(
        "tkh,tkl->thl", coded_high, low_hot.astype(jnp.bfloat16), preferred_element_type=jnp.float32
    )
    spread = spread.astype(jnp.bfloat16).reshape(tokens, range_size)
    half = weights.shape[1] // 2
    w_first, w_second = weights[:, :half], weights[:, half:]
    partial_first = jnp.dot(spread, w_first, preferred_element_type=jnp.float32).astype(jnp.bfloat16)
    decoded_first = lax.psum_scatter(partial_first, "tok", scatter_dimension=0, tiled=True)
    partial_second = jnp.dot(spread, w_second, preferred_element_type=jnp.float32).astype(jnp.bfloat16)
    received = lax.all_to_all(partial_second, "tok", split_axis=0, concat_axis=0, tiled=True)
    decoded_second = jnp.sum(
        received.reshape(owners, -1, received.shape[1]).astype(jnp.float32), axis=0
    )
    decoded = jnp.concatenate([decoded_first.astype(jnp.float32), decoded_second], axis=1)
    recon_full, grad_sum = layer_chain(decoded, carry_gain, earlier_sum, targets)
    grad_low = grad_sum.astype(jnp.bfloat16)
    segment = lax.all_gather(grad_low, "tok", axis=0, tiled=True)
    products = lax.dot_general(
        segment, weights, (((1,), (1,)), ((), ())), preferred_element_type=jnp.float32
    ).astype(jnp.bfloat16)
    products = products.reshape(tokens, range_size // LANES, LANES)
    picked_low = jnp.einsum(
        "thl,tkl->tkh",
        products,
        low_hot.astype(jnp.bfloat16),
        preferred_element_type=jnp.float32,
    )
    partial_grad = jnp.sum(jnp.where(high_hot, picked_low, 0.0), axis=-1)
    returned = lax.all_to_all(partial_grad, "tok", split_axis=0, concat_axis=0, tiled=True)
    code_grad = jnp.sum(returned.reshape(owners, -1, returned.shape[1]), axis=0)
    return (recon_full.astype(jnp.bfloat16)[None], code_grad[None])


def solution(mesh):
    return jax.shard_map(
        on_device,
        mesh=mesh,
        in_specs=(
            P("layer", "tok", None),
            P("layer", "tok", None),
            P("layer", "tok", None),
            P("layer", None),
            P("tok", None),
            P("layer", "tok", None),
        ),
        out_specs=(P("layer", "tok", None), P("layer", "tok", None)),
        check_vma=False,
    )
```

```python
import jax
import jax.numpy as jnp
from jax import lax
from jax.sharding import PartitionSpec as P

LANES = 128


def selectors(ids_all, range_size):
    base = lax.axis_index("tok") * range_size
    local = ids_all - base
    inside = (local >= 0) & (local < range_size)
    high = jnp.where(inside, local // LANES, -1)
    low = local % LANES
    high_hot = high[..., None] == jnp.arange(range_size // LANES, dtype=jnp.int32)
    low_hot = low[..., None] == jnp.arange(LANES, dtype=jnp.int32)
    return high_hot, low_hot


def exchange_codes(latent_ids, active_codes):
    owners = lax.axis_size("tok")
    top_count = latent_ids.shape[1]
    packed = jnp.concatenate(
        [latent_ids.astype(jnp.float32), active_codes.astype(jnp.float32)], axis=1
    )
    spread = jnp.broadcast_to(packed[None], (owners,) + packed.shape)
    gathered = lax.all_to_all(spread, "tok", split_axis=0, concat_axis=0, tiled=True)
    gathered = gathered.reshape(-1, 2 * top_count)
    ids_all = gathered[:, :top_count].astype(jnp.int32)
    codes_all = gathered[:, top_count:].astype(jnp.bfloat16)
    return ids_all, codes_all


def layer_chain(decoded, carry_gain, earlier_sum, targets):
    gains = lax.all_gather(carry_gain[0], "layer", axis=0, tiled=False)
    targets_all = lax.all_gather(targets[0], "layer", axis=0, tiled=False)
    decoded_all = lax.all_gather(decoded.astype(jnp.bfloat16), "layer", axis=0, tiled=False)
    layers = gains.shape[0]
    me = lax.axis_index("layer")
    carried = earlier_sum.astype(jnp.float32)
    misfits = []
    recon_own = jnp.zeros_like(decoded)
    for m in range(layers):
        own = me == m
        term = jnp.where(own, decoded, decoded_all[m].astype(jnp.float32))
        carried = term + gains[m][None, :] * carried
        recon_own = jnp.where(own, carried, recon_own)
        misfits.append(carried - targets_all[m].astype(jnp.float32))
    running = misfits[layers - 1]
    grad_own = jnp.where(me == layers - 1, running, jnp.zeros_like(running))
    for m in range(layers - 2, -1, -1):
        running = misfits[m] + gains[m + 1][None, :] * running
        grad_own = jnp.where(me == m, running, grad_own)
    return recon_own, grad_own


def on_device(active_codes, latent_ids, decoder, carry_gain, earlier_sum, targets):
    range_size = decoder.shape[1]
    owners = lax.axis_size("tok")
    weights = decoder[0]
    ids_all, codes_all = exchange_codes(latent_ids[0], active_codes[0])
    tokens = ids_all.shape[0]
    high_hot, low_hot = selectors(ids_all, range_size)
    coded_high = jnp.where(high_hot, codes_all[..., None], jnp.zeros((), jnp.bfloat16))
    spread = jnp.einsum(
        "tkh,tkl->thl", coded_high, low_hot.astype(jnp.bfloat16), preferred_element_type=jnp.float32
    )
    spread = spread.astype(jnp.bfloat16).reshape(tokens, range_size)
    width = weights.shape[1]
    half = (5 * width // 8) // LANES * LANES if width % (8 * LANES) == 0 else width // 2
    w_first, w_second = weights[:, :half], weights[:, half:]
    partial_first = jnp.dot(spread, w_first, preferred_element_type=jnp.float32).astype(jnp.bfloat16)
    decoded_first = lax.psum_scatter(partial_first, "tok", scatter_dimension=0, tiled=True)
    partial_first, spread = lax.optimization_barrier((partial_first, spread))
    partial_second = jnp.dot(spread, w_second, preferred_element_type=jnp.float32).astype(jnp.bfloat16)
    received = lax.all_to_all(partial_second, "tok", split_axis=0, concat_axis=0, tiled=True)
    decoded_second = jnp.sum(
        received.reshape(owners, -1, received.shape[1]).astype(jnp.float32), axis=0
    )
    decoded = jnp.concatenate([decoded_first.astype(jnp.float32), decoded_second], axis=1)
    recon_full, grad_sum = layer_chain(decoded, carry_gain, earlier_sum, targets)
    grad_low = grad_sum.astype(jnp.bfloat16)
    segment = lax.all_gather(grad_low, "tok", axis=0, tiled=True)
    products = lax.dot_general(
        segment, weights, (((1,), (1,)), ((), ())), preferred_element_type=jnp.float32
    ).astype(jnp.bfloat16)
    products = products.reshape(tokens, range_size // LANES, LANES)
    picked_low = jnp.einsum(
        "thl,tkl->tkh",
        products,
        low_hot.astype(jnp.bfloat16),
        preferred_element_type=jnp.float32,
    )
    partial_grad = jnp.sum(jnp.where(high_hot, picked_low, 0.0), axis=-1)
    returned = lax.all_to_all(partial_grad, "tok", split_axis=0, concat_axis=0, tiled=True)
    code_grad = jnp.sum(returned.reshape(owners, -1, returned.shape[1]), axis=0)
    return (recon_full.astype(jnp.bfloat16)[None], code_grad[None])


def solution(mesh):
    return jax.shard_map(
        on_device,
        mesh=mesh,
        in_specs=(
            P("layer", "tok", None),
            P("layer", "tok", None),
            P("layer", "tok", None),
            P("layer", None),
            P("tok", None),
            P("layer", "tok", None),
        ),
        out_specs=(P("layer", "tok", None), P("layer", "tok", None)),
        check_vma=False,
    )
```

```python
import functools

import jax
import jax.numpy as jnp
from jax import lax
from jax.sharding import PartitionSpec as P

LANES = 128


def selectors(ids_all, range_size):
    base = lax.axis_index("tok") * range_size
    local = ids_all - base
    inside = (local >= 0) & (local < range_size)
    high = jnp.where(inside, local // LANES, -1)
    low = local % LANES
    high_hot = high[..., None] == jnp.arange(range_size // LANES, dtype=jnp.int32)
    low_hot = low[..., None] == jnp.arange(LANES, dtype=jnp.int32)
    return high_hot, low_hot


def ring_order(mesh):
    count = mesh.shape["tok"]
    row = mesh.devices.reshape(-1, count)[0]
    coords = [getattr(device, "coords", None) for device in row]
    if any(c is None for c in coords):
        return list(range(count))
    varying = [d for d in range(len(coords[0])) if len({c[d] for c in coords}) > 1]
    if len(varying) != 2:
        return sorted(range(count), key=lambda i: tuple(coords[i]))
    sizes = [len({c[d] for c in coords}) for d in varying]
    outer, inner = (1, 0) if sizes[1] % 2 == 0 else (0, 1)
    place = {(coords[i][varying[outer]], coords[i][varying[inner]]): i for i in range(count)}
    outer_values = sorted({c[varying[outer]] for c in coords})
    inner_values = sorted({c[varying[inner]] for c in coords})
    order = []
    for n, o in enumerate(outer_values):
        walk = inner_values if n % 2 == 0 else inner_values[::-1]
        order.extend(place[(o, i)] for i in walk)
    return order


def ring_tables(ring):
    count = len(ring)
    position = [0] * count
    for p, i in enumerate(ring):
        position[i] = p
    forward = [(ring[p], ring[(p + 1) % count]) for p in range(count)]
    backward = [(ring[(p + 1) % count], ring[p]) for p in range(count)]
    here = jnp.asarray(position, jnp.int32)[lax.axis_index("tok")]
    return jnp.asarray(ring, jnp.int32), here, forward, backward


def ring_reduce_scatter(partial, ring):
    count = len(ring)
    members, here, forward, backward = ring_tables(ring)
    blocks = partial.reshape(count, -1, partial.shape[1])
    half = partial.shape[1] // 2
    sides = ((forward, -1, slice(0, half)), (backward, 1, slice(half, None)))
    results = []
    for perm, sign, cols in sides:
        own = blocks[:, :, cols]
        first = lax.dynamic_index_in_dim(own, members[(here + sign) % count], 0, keepdims=False)
        running = first
        for s in range(count - 1):
            arrived = lax.ppermute(running, "tok", perm)
            block = members[(here + sign * (s + 2)) % count]
            total = arrived.astype(jnp.float32) + lax.dynamic_index_in_dim(
                own, block, 0, keepdims=False
            ).astype(jnp.float32)
            running = total.astype(jnp.bfloat16)
        results.append(total)
    return jnp.concatenate(results, axis=1)


def exchange_codes(latent_ids, active_codes):
    owners = lax.axis_size("tok")
    top_count = latent_ids.shape[1]
    packed = jnp.concatenate(
        [latent_ids.astype(jnp.float32), active_codes.astype(jnp.float32)], axis=1
    )
    spread = jnp.broadcast_to(packed[None], (owners,) + packed.shape)
    gathered = lax.all_to_all(spread, "tok", split_axis=0, concat_axis=0, tiled=True)
    gathered = gathered.reshape(-1, 2 * top_count)
    ids_all = gathered[:, :top_count].astype(jnp.int32)
    codes_all = gathered[:, top_count:].astype(jnp.bfloat16)
    return ids_all, codes_all


def layer_chain(decoded, carry_gain, earlier_sum, targets):
    gains = lax.all_gather(carry_gain[0], "layer", axis=0, tiled=False)
    targets_all = lax.all_gather(targets[0], "layer", axis=0, tiled=False)
    decoded_all = lax.all_gather(decoded.astype(jnp.bfloat16), "layer", axis=0, tiled=False)
    layers = gains.shape[0]
    me = lax.axis_index("layer")
    carried = earlier_sum.astype(jnp.float32)
    misfits = []
    recon_own = jnp.zeros_like(decoded)
    for m in range(layers):
        own = me == m
        term = jnp.where(own, decoded, decoded_all[m].astype(jnp.float32))
        carried = term + gains[m][None, :] * carried
        recon_own = jnp.where(own, carried, recon_own)
        misfits.append(carried - targets_all[m].astype(jnp.float32))
    running = misfits[layers - 1]
    grad_own = jnp.where(me == layers - 1, running, jnp.zeros_like(running))
    for m in range(layers - 2, -1, -1):
        running = misfits[m] + gains[m + 1][None, :] * running
        grad_own = jnp.where(me == m, running, grad_own)
    return recon_own, grad_own


def on_device(ring, active_codes, latent_ids, decoder, carry_gain, earlier_sum, targets):
    range_size = decoder.shape[1]
    owners = lax.axis_size("tok")
    weights = decoder[0]
    ids_all, codes_all = exchange_codes(latent_ids[0], active_codes[0])
    tokens = ids_all.shape[0]
    high_hot, low_hot = selectors(ids_all, range_size)
    coded_high = jnp.where(high_hot, codes_all[..., None], jnp.zeros((), jnp.bfloat16))
    spread = jnp.einsum(
        "tkh,tkl->thl", coded_high, low_hot.astype(jnp.bfloat16), preferred_element_type=jnp.float32
    )
    spread = spread.astype(jnp.bfloat16).reshape(tokens, range_size)
    half = weights.shape[1] // 2
    w_first, w_second = weights[:, :half], weights[:, half:]
    partial_first = jnp.dot(spread, w_first, preferred_element_type=jnp.float32).astype(jnp.bfloat16)
    decoded_first = lax.psum_scatter(partial_first, "tok", scatter_dimension=0, tiled=True)
    partial_second = jnp.dot(spread, w_second, preferred_element_type=jnp.float32).astype(jnp.bfloat16)
    decoded_second = ring_reduce_scatter(partial_second, ring)
    decoded = jnp.concatenate([decoded_first.astype(jnp.float32), decoded_second], axis=1)
    recon_full, grad_sum = layer_chain(decoded, carry_gain, earlier_sum, targets)
    grad_low = grad_sum.astype(jnp.bfloat16)
    segment = lax.all_gather(grad_low, "tok", axis=0, tiled=True)
    products = lax.dot_general(
        segment, weights, (((1,), (1,)), ((), ())), preferred_element_type=jnp.float32
    ).astype(jnp.bfloat16)
    products = products.reshape(tokens, range_size // LANES, LANES)
    picked_low = jnp.einsum(
        "thl,tkl->tkh",
        products,
        low_hot.astype(jnp.bfloat16),
        preferred_element_type=jnp.float32,
    )
    partial_grad = jnp.sum(jnp.where(high_hot, picked_low, 0.0), axis=-1)
    returned = lax.all_to_all(partial_grad, "tok", split_axis=0, concat_axis=0, tiled=True)
    code_grad = jnp.sum(returned.reshape(owners, -1, returned.shape[1]), axis=0)
    return (recon_full.astype(jnp.bfloat16)[None], code_grad[None])


def solution(mesh):
    ring = ring_order(mesh)
    return jax.shard_map(
        functools.partial(on_device, ring),
        mesh=mesh,
        in_specs=(
            P("layer", "tok", None),
            P("layer", "tok", None),
            P("layer", "tok", None),
            P("layer", None),
            P("tok", None),
            P("layer", "tok", None),
        ),
        out_specs=(P("layer", "tok", None), P("layer", "tok", None)),
        check_vma=False,
    )
```

```python
import functools

import jax
import jax.numpy as jnp
from jax import lax
from jax.sharding import PartitionSpec as P

LANES = 128


def selectors(ids_all, range_size):
    base = lax.axis_index("tok") * range_size
    local = ids_all - base
    inside = (local >= 0) & (local < range_size)
    high = jnp.where(inside, local // LANES, -1)
    low = local % LANES
    high_hot = high[..., None] == jnp.arange(range_size // LANES, dtype=jnp.int32)
    low_hot = low[..., None] == jnp.arange(LANES, dtype=jnp.int32)
    return high_hot, low_hot


def ring_order(mesh):
    count = mesh.shape["tok"]
    row = mesh.devices.reshape(-1, count)[0]
    coords = [getattr(device, "coords", None) for device in row]
    if any(c is None for c in coords):
        return list(range(count))
    varying = [d for d in range(len(coords[0])) if len({c[d] for c in coords}) > 1]
    if len(varying) != 2:
        return sorted(range(count), key=lambda i: tuple(coords[i]))
    sizes = [len({c[d] for c in coords}) for d in varying]
    outer, inner = (1, 0) if sizes[1] % 2 == 0 else (0, 1)
    place = {(coords[i][varying[outer]], coords[i][varying[inner]]): i for i in range(count)}
    outer_values = sorted({c[varying[outer]] for c in coords})
    inner_values = sorted({c[varying[inner]] for c in coords})
    order = []
    for n, o in enumerate(outer_values):
        walk = inner_values if n % 2 == 0 else inner_values[::-1]
        order.extend(place[(o, i)] for i in walk)
    return order


def ring_tables(ring):
    count = len(ring)
    position = [0] * count
    for p, i in enumerate(ring):
        position[i] = p
    forward = [(ring[p], ring[(p + 1) % count]) for p in range(count)]
    backward = [(ring[(p + 1) % count], ring[p]) for p in range(count)]
    here = jnp.asarray(position, jnp.int32)[lax.axis_index("tok")]
    return jnp.asarray(ring, jnp.int32), here, forward, backward


def ring_all_gather(piece, ring):
    count = len(ring)
    members, here, forward, backward = ring_tables(ring)
    half = piece.shape[1] // 2
    gathered = jnp.zeros((count,) + piece.shape, piece.dtype)
    me = lax.axis_index("tok")
    gathered = lax.dynamic_update_index_in_dim(gathered, piece, me, 0)
    sides = ((forward, -1, 0, piece[:, :half]), (backward, 1, half, piece[:, half:]))
    for perm, sign, offset, travelling in sides:
        for s in range(count - 1):
            travelling = lax.ppermute(travelling, "tok", perm)
            source = members[(here + sign * (s + 1)) % count]
            gathered = lax.dynamic_update_slice(
                gathered, travelling[None], (source, jnp.int32(0), jnp.int32(offset))
            )
    return gathered.reshape(count * piece.shape[0], piece.shape[1])


def exchange_codes(latent_ids, active_codes):
    owners = lax.axis_size("tok")
    top_count = latent_ids.shape[1]
    packed = jnp.concatenate(
        [latent_ids.astype(jnp.float32), active_codes.astype(jnp.float32)], axis=1
    )
    spread = jnp.broadcast_to(packed[None], (owners,) + packed.shape)
    gathered = lax.all_to_all(spread, "tok", split_axis=0, concat_axis=0, tiled=True)
    gathered = gathered.reshape(-1, 2 * top_count)
    ids_all = gathered[:, :top_count].astype(jnp.int32)
    codes_all = gathered[:, top_count:].astype(jnp.bfloat16)
    return ids_all, codes_all


def layer_chain(decoded, carry_gain, earlier_sum, targets):
    gains = lax.all_gather(carry_gain[0], "layer", axis=0, tiled=False)
    targets_all = lax.all_gather(targets[0], "layer", axis=0, tiled=False)
    decoded_all = lax.all_gather(decoded.astype(jnp.bfloat16), "layer", axis=0, tiled=False)
    layers = gains.shape[0]
    me = lax.axis_index("layer")
    carried = earlier_sum.astype(jnp.float32)
    misfits = []
    recon_own = jnp.zeros_like(decoded)
    for m in range(layers):
        own = me == m
        term = jnp.where(own, decoded, decoded_all[m].astype(jnp.float32))
        carried = term + gains[m][None, :] * carried
        recon_own = jnp.where(own, carried, recon_own)
        misfits.append(carried - targets_all[m].astype(jnp.float32))
    running = misfits[layers - 1]
    grad_own = jnp.where(me == layers - 1, running, jnp.zeros_like(running))
    for m in range(layers - 2, -1, -1):
        running = misfits[m] + gains[m + 1][None, :] * running
        grad_own = jnp.where(me == m, running, grad_own)
    return recon_own, grad_own


def on_device(ring, active_codes, latent_ids, decoder, carry_gain, earlier_sum, targets):
    range_size = decoder.shape[1]
    owners = lax.axis_size("tok")
    weights = decoder[0]
    ids_all, codes_all = exchange_codes(latent_ids[0], active_codes[0])
    tokens = ids_all.shape[0]
    high_hot, low_hot = selectors(ids_all, range_size)
    coded_high = jnp.where(high_hot, codes_all[..., None], jnp.zeros((), jnp.bfloat16))
    spread = jnp.einsum(
        "tkh,tkl->thl", coded_high, low_hot.astype(jnp.bfloat16), preferred_element_type=jnp.float32
    )
    spread = spread.astype(jnp.bfloat16).reshape(tokens, range_size)
    width = weights.shape[1]
    half = width // 2
    w_first, w_second = weights[:, :half], weights[:, half:]
    partial_first = jnp.dot(spread, w_first, preferred_element_type=jnp.float32).astype(jnp.bfloat16)
    decoded_first = lax.psum_scatter(partial_first, "tok", scatter_dimension=0, tiled=True)
    partial_second = jnp.dot(spread, w_second, preferred_element_type=jnp.float32).astype(jnp.bfloat16)
    received = lax.all_to_all(partial_second, "tok", split_axis=0, concat_axis=0, tiled=True)
    decoded_second = jnp.sum(
        received.reshape(owners, -1, received.shape[1]).astype(jnp.float32), axis=0
    )
    decoded = jnp.concatenate([decoded_first.astype(jnp.float32), decoded_second], axis=1)
    recon_full, grad_sum = layer_chain(decoded, carry_gain, earlier_sum, targets)
    grad_low = grad_sum.astype(jnp.bfloat16)
    split = 3 * width // 4 if width % (4 * LANES) == 0 else width // 2
    segment = jnp.concatenate(
        [
            lax.all_gather(grad_low[:, :split], "tok", axis=0, tiled=True),
            ring_all_gather(grad_low[:, split:], ring),
        ],
        axis=1,
    )
    products = lax.dot_general(
        segment, weights, (((1,), (1,)), ((), ())), preferred_element_type=jnp.float32
    ).astype(jnp.bfloat16)
    products = products.reshape(tokens, range_size // LANES, LANES)
    picked_low = jnp.einsum(
        "thl,tkl->tkh",
        products,
        low_hot.astype(jnp.bfloat16),
        preferred_element_type=jnp.float32,
    )
    partial_grad = jnp.sum(jnp.where(high_hot, picked_low, 0.0), axis=-1)
    returned = lax.all_to_all(partial_grad, "tok", split_axis=0, concat_axis=0, tiled=True)
    code_grad = jnp.sum(returned.reshape(owners, -1, returned.shape[1]), axis=0)
    return (recon_full.astype(jnp.bfloat16)[None], code_grad[None])


def solution(mesh):
    ring = ring_order(mesh)
    return jax.shard_map(
        functools.partial(on_device, ring),
        mesh=mesh,
        in_specs=(
            P("layer", "tok", None),
            P("layer", "tok", None),
            P("layer", "tok", None),
            P("layer", None),
            P("tok", None),
            P("layer", "tok", None),
        ),
        out_specs=(P("layer", "tok", None), P("layer", "tok", None)),
        check_vma=False,
    )
```

```python
import jax
import jax.numpy as jnp
from jax import lax
from jax.sharding import PartitionSpec as P

LANES = 128


def selectors(ids_all, range_size):
    base = lax.axis_index("tok") * range_size
    local = ids_all - base
    inside = (local >= 0) & (local < range_size)
    high = jnp.where(inside, local // LANES, -1)
    low = local % LANES
    high_hot = high[..., None] == jnp.arange(range_size // LANES, dtype=jnp.int32)
    low_hot = low[..., None] == jnp.arange(LANES, dtype=jnp.int32)
    return high_hot, low_hot


def exchange_codes(latent_ids, active_codes):
    owners = lax.axis_size("tok")
    top_count = latent_ids.shape[1]
    packed = jnp.concatenate(
        [latent_ids.astype(jnp.float32), active_codes.astype(jnp.float32)], axis=1
    )
    spread = jnp.broadcast_to(packed[None], (owners,) + packed.shape)
    gathered = lax.all_to_all(spread, "tok", split_axis=0, concat_axis=0, tiled=True)
    gathered = gathered.reshape(-1, 2 * top_count)
    ids_all = gathered[:, :top_count].astype(jnp.int32)
    codes_all = gathered[:, top_count:].astype(jnp.bfloat16)
    return ids_all, codes_all


def layer_chain(decoded, carry_gain, earlier_sum, targets):
    gains = lax.all_gather(carry_gain[0], "layer", axis=0, tiled=False)
    targets_all = lax.all_gather(targets[0], "layer", axis=0, tiled=False)
    layers = gains.shape[0]
    me = lax.axis_index("layer")
    one = jnp.ones_like(gains[0])
    zero = jnp.zeros_like(gains[0])

    def span(first, last):
        product = one
        for i in range(first, last + 1):
            product = product * gains[i]
        return product

    def pick(values):
        chosen = zero
        for l, value in enumerate(values):
            chosen = jnp.where(me == l, value, chosen)
        return chosen

    def ahead(l, m):
        return span(l + 1, m) if m >= l else zero

    recon_weight = [pick([span(n + 1, l) if n <= l else zero for l in range(layers)]) for n in range(layers)]
    earlier_weight = pick([span(0, l) for l in range(layers)])
    grad_weight = [
        pick([sum(ahead(l, m) * span(n + 1, m) for m in range(max(l, n), layers)) for l in range(layers)])
        for n in range(layers)
    ]
    grad_earlier = pick([sum(ahead(l, m) * span(0, m) for m in range(l, layers)) for l in range(layers)])
    target_weight = [pick([ahead(l, m) for l in range(layers)]) for m in range(layers)]
    early = grad_earlier[None, :] * earlier_sum.astype(jnp.float32)
    for m in range(layers):
        early = early - target_weight[m][None, :] * targets_all[m].astype(jnp.float32)
    decoded_all = lax.all_gather(decoded.astype(jnp.bfloat16), "layer", axis=0, tiled=False)
    terms = [
        jnp.where(me == n, decoded, decoded_all[n].astype(jnp.float32)) for n in range(layers)
    ]
    grad_own = early
    recon_own = earlier_weight[None, :] * earlier_sum.astype(jnp.float32)
    for n in range(layers):
        grad_own = grad_own + grad_weight[n][None, :] * terms[n]
        recon_own = recon_own + recon_weight[n][None, :] * terms[n]
    return recon_own, grad_own

def on_device(active_codes, latent_ids, decoder, carry_gain, earlier_sum, targets):
    range_size = decoder.shape[1]
    owners = lax.axis_size("tok")
    weights = decoder[0]
    ids_all, codes_all = exchange_codes(latent_ids[0], active_codes[0])
    tokens = ids_all.shape[0]
    high_hot, low_hot = selectors(ids_all, range_size)
    coded_high = jnp.where(high_hot, codes_all[..., None], jnp.zeros((), jnp.bfloat16))
    spread = jnp.einsum(
        "tkh,tkl->thl", coded_high, low_hot.astype(jnp.bfloat16), preferred_element_type=jnp.float32
    )
    spread = spread.astype(jnp.bfloat16).reshape(tokens, range_size)
    half = weights.shape[1] // 2
    w_first, w_second = weights[:, :half], weights[:, half:]
    partial_first = jnp.dot(spread, w_first, preferred_element_type=jnp.float32).astype(jnp.bfloat16)
    decoded_first = lax.psum_scatter(partial_first, "tok", scatter_dimension=0, tiled=True)
    partial_second = jnp.dot(spread, w_second, preferred_element_type=jnp.float32).astype(jnp.bfloat16)
    received = lax.all_to_all(partial_second, "tok", split_axis=0, concat_axis=0, tiled=True)
    decoded_second = jnp.sum(
        received.reshape(owners, -1, received.shape[1]).astype(jnp.float32), axis=0
    )
    decoded = jnp.concatenate([decoded_first.astype(jnp.float32), decoded_second], axis=1)
    recon_full, grad_sum = layer_chain(decoded, carry_gain, earlier_sum, targets)
    grad_low = grad_sum.astype(jnp.bfloat16)
    segment = lax.all_gather(grad_low, "tok", axis=0, tiled=True)
    products = lax.dot_general(
        segment, weights, (((1,), (1,)), ((), ())), preferred_element_type=jnp.float32
    ).astype(jnp.bfloat16)
    products = products.reshape(tokens, range_size // LANES, LANES)
    picked_low = jnp.einsum(
        "thl,tkl->tkh",
        products,
        low_hot.astype(jnp.bfloat16),
        preferred_element_type=jnp.float32,
    )
    partial_grad = jnp.sum(jnp.where(high_hot, picked_low, 0.0), axis=-1)
    returned = lax.all_to_all(partial_grad, "tok", split_axis=0, concat_axis=0, tiled=True)
    code_grad = jnp.sum(returned.reshape(owners, -1, returned.shape[1]), axis=0)
    return (recon_full.astype(jnp.bfloat16)[None], code_grad[None])


def solution(mesh):
    return jax.shard_map(
        on_device,
        mesh=mesh,
        in_specs=(
            P("layer", "tok", None),
            P("layer", "tok", None),
            P("layer", "tok", None),
            P("layer", None),
            P("tok", None),
            P("layer", "tok", None),
        ),
        out_specs=(P("layer", "tok", None), P("layer", "tok", None)),
        check_vma=False,
    )
```

```python
import jax
import jax.numpy as jnp
from jax import lax
from jax.sharding import PartitionSpec as P

LANES = 128


def selectors(ids_all, range_size):
    base = lax.axis_index("tok") * range_size
    local = ids_all - base
    inside = (local >= 0) & (local < range_size)
    high = jnp.where(inside, local // LANES, -1)
    low = local % LANES
    high_hot = high[..., None] == jnp.arange(range_size // LANES, dtype=jnp.int32)
    low_hot = low[..., None] == jnp.arange(LANES, dtype=jnp.int32)
    return high_hot, low_hot


def exchange_codes(latent_ids, active_codes):
    owners = lax.axis_size("tok")
    top_count = latent_ids.shape[1]
    packed = jnp.concatenate(
        [
            (latent_ids // 256).astype(jnp.bfloat16),
            (latent_ids % 256).astype(jnp.bfloat16),
            active_codes,
        ],
        axis=1,
    )
    spread = jnp.broadcast_to(packed[None], (owners,) + packed.shape)
    gathered = lax.all_to_all(spread, "tok", split_axis=0, concat_axis=0, tiled=True)
    gathered = gathered.reshape(-1, 3 * top_count)
    ids_all = gathered[:, :top_count].astype(jnp.int32) * 256 + gathered[
        :, top_count:2 * top_count
    ].astype(jnp.int32)
    codes_all = gathered[:, 2 * top_count:]
    return ids_all, codes_all


def layer_chain(decoded, carry_gain, earlier_sum, targets):
    gains = lax.all_gather(carry_gain[0], "layer", axis=0, tiled=False)
    targets_all = lax.all_gather(targets[0], "layer", axis=0, tiled=False)
    decoded_all = lax.all_gather(decoded.astype(jnp.bfloat16), "layer", axis=0, tiled=False)
    layers = gains.shape[0]
    me = lax.axis_index("layer")
    carried = earlier_sum.astype(jnp.float32)
    misfits = []
    recon_own = jnp.zeros_like(decoded)
    for m in range(layers):
        own = me == m
        term = jnp.where(own, decoded, decoded_all[m].astype(jnp.float32))
        carried = term + gains[m][None, :] * carried
        recon_own = jnp.where(own, carried, recon_own)
        misfits.append(carried - targets_all[m].astype(jnp.float32))
    running = misfits[layers - 1]
    grad_own = jnp.where(me == layers - 1, running, jnp.zeros_like(running))
    for m in range(layers - 2, -1, -1):
        running = misfits[m] + gains[m + 1][None, :] * running
        grad_own = jnp.where(me == m, running, grad_own)
    return recon_own, grad_own


def on_device(active_codes, latent_ids, decoder, carry_gain, earlier_sum, targets):
    range_size = decoder.shape[1]
    owners = lax.axis_size("tok")
    weights = decoder[0]
    ids_all, codes_all = exchange_codes(latent_ids[0], active_codes[0])
    tokens = ids_all.shape[0]
    high_hot, low_hot = selectors(ids_all, range_size)
    coded_high = jnp.where(high_hot, codes_all[..., None], jnp.zeros((), jnp.bfloat16))
    spread = jnp.einsum(
        "tkh,tkl->thl", coded_high, low_hot.astype(jnp.bfloat16), preferred_element_type=jnp.float32
    )
    spread = spread.astype(jnp.bfloat16).reshape(tokens, range_size)
    half = weights.shape[1] // 2
    w_first, w_second = weights[:, :half], weights[:, half:]
    partial_first = jnp.dot(spread, w_first, preferred_element_type=jnp.float32).astype(jnp.bfloat16)
    decoded_first = lax.psum_scatter(partial_first, "tok", scatter_dimension=0, tiled=True)
    partial_second = jnp.dot(spread, w_second, preferred_element_type=jnp.float32).astype(jnp.bfloat16)
    received = lax.all_to_all(partial_second, "tok", split_axis=0, concat_axis=0, tiled=True)
    decoded_second = jnp.sum(
        received.reshape(owners, -1, received.shape[1]).astype(jnp.float32), axis=0
    )
    decoded = jnp.concatenate([decoded_first.astype(jnp.float32), decoded_second], axis=1)
    recon_full, grad_sum = layer_chain(decoded, carry_gain, earlier_sum, targets)
    grad_low = grad_sum.astype(jnp.bfloat16)
    segment = lax.all_gather(grad_low, "tok", axis=0, tiled=True)
    products = lax.dot_general(
        segment, weights, (((1,), (1,)), ((), ())), preferred_element_type=jnp.float32
    ).astype(jnp.bfloat16)
    products = products.reshape(tokens, range_size // LANES, LANES)
    picked_low = jnp.einsum(
        "thl,tkl->tkh",
        products,
        low_hot.astype(jnp.bfloat16),
        preferred_element_type=jnp.float32,
    )
    partial_grad = jnp.sum(jnp.where(high_hot, picked_low, 0.0), axis=-1)
    returned = lax.all_to_all(partial_grad, "tok", split_axis=0, concat_axis=0, tiled=True)
    code_grad = jnp.sum(returned.reshape(owners, -1, returned.shape[1]), axis=0)
    return (recon_full.astype(jnp.bfloat16)[None], code_grad[None])


def solution(mesh):
    return jax.shard_map(
        on_device,
        mesh=mesh,
        in_specs=(
            P("layer", "tok", None),
            P("layer", "tok", None),
            P("layer", "tok", None),
            P("layer", None),
            P("tok", None),
            P("layer", "tok", None),
        ),
        out_specs=(P("layer", "tok", None), P("layer", "tok", None)),
        check_vma=False,
    )
```
